256 devices in a mesh: dp: 8 (over x, core), ctx: 32 (over z, y).
Axes of the slice: x: 4, y: 4, z: 8, core: 2. Of those that a mesh axis runs over, the one named last changes fastest.
Arguments:
- query_proj: bfloat16 [8, 4096, 4096], P('dp', 'ctx'), may hold values from -6 to 6
- key_proj: bfloat16 [8, 4096, 4096], P('dp', 'ctx'), may hold values from -6 to 6
- value_proj: bfloat16 [8, 4096, 4096], P('dp', 'ctx'), may hold values from -6 to 6
- doc_offset: int32 [8, 4096], P('dp', 'ctx'), may hold values from 0 to 4095, as said below
- short_taps: float32 [3, 7, 4096], replicated, may hold values from -2.5 to 2.5
- rate_scale: float32 [16, 4096], replicated, may hold values from 0.1 to 120
- residue: float32 [16, 4096], replicated, may hold values from -2.5 to 2.5
- skip_gain: float32 [4096], replicated, may hold values from 0.5 to 1.5
- out_grad: bfloat16 [8, 4096, 4096], P('dp', 'ctx'), may hold values from -6 to 6
Outputs:
- mixed_out: bfloat16 [8, 4096, 4096], P('dp', 'ctx')
- query_grad: bfloat16 [8, 4096, 4096], P('dp', 'ctx')
- key_grad: bfloat16 [8, 4096, 4096], P('dp', 'ctx')
- value_grad: bfloat16 [8, 4096, 4096], P('dp', 'ctx')
- taps_grad: float32 [3, 7, 4096], replicated
- skip_grad: float32 [4096], replicated
- residue_grad: float32 [16, 4096], replicated
The draws below stay inside these ranges and needn't reach their ends.
Inputs may be any that keep to these rules, and one draw needn't show every extreme that they name: `doc_offset`: each row is a run of whole documents: the value is a token's index inside its document, 0 at a document's first position and rising by one along it. The first row holds a single document.
All inputs are finite; a program needn't handle non-finite values.
Results may differ from the reference program's by a relative error of at most 0.0013.
Values may be sent and summed in bfloat16 or wider, within the bound.
No kernel may reach another device: no remote copies, remote signals or barrier semaphores. Data moves between devices by JAX's collectives and lax.ppermute only.
A program may use at most 192 MiB of HBM per device.

```python
import math
import jax
import jax.numpy as jnp
from jax import lax

CH = 4096
ORDER = 16
TAPS = 7
SEQ = 4096
ROWS = 8


def draw_doc_offset(key, part):
    starts = jax.random.randint(key, (ROWS, SEQ), 0, SEQ) < 4
    positions = jnp.broadcast_to(jnp.arange(SEQ, dtype=jnp.int32)[None, :], (ROWS, SEQ))
    single_doc = jnp.arange(ROWS, dtype=jnp.int32)[:, None] == 0
    starts = jnp.logical_and(starts, jnp.logical_not(single_doc))
    starts = jnp.logical_or(starts, positions == 0)
    last_start = lax.cummax(jnp.where(starts, positions, 0), axis=1)
    return (positions - last_start).astype(jnp.int32)


def shard_levels(rng, dims, cuts, low, top_value):
    loudness, own = 1.0, jax.random.fold_in(rng, 6)
    for axis_at, blocks in cuts:
        draws = jnp.exp(jax.random.uniform(jax.random.fold_in(own, axis_at), (blocks,), jnp.float32, low / len(cuts), top_value / len(cuts)))
        loudness = loudness * jnp.repeat(draws, dims[axis_at] // blocks).reshape([-1 if axis == axis_at else 1 for axis in range(len(dims))])
    return loudness


def normal_values(key, dims, width, bound, split=(), held_as=jnp.bfloat16):
    result = jax.random.normal(key, dims, jnp.float32) * width
    if len(split) > 0:
        result = shard_levels(key, dims, split, -0.22, 0.18) * result
    return jnp.clip(result, min=-bound, max=bound).astype(held_as)


def setup_inputs(seed: int = 0) -> dict:
    streams_of = jax.random.split(jax.random.key(seed), 10)
    return {
        "query_proj": normal_values(streams_of[0], (ROWS, SEQ, CH), 1.0, 6.0, ((0, 8), (1, 32))),
        "key_proj": normal_values(streams_of[1], (ROWS, SEQ, CH), 1.0, 6.0, ((0, 8), (1, 32))),
        "value_proj": normal_values(streams_of[2], (ROWS, SEQ, CH), 1.0, 6.0, ((0, 8), (1, 32))),
        "doc_offset": draw_doc_offset(jax.random.fold_in(streams_of[9], 71), 0),
        "short_taps": normal_values(streams_of[4], (3, TAPS, CH), 0.4, 2.5, (), jnp.float32),
        "rate_scale": jnp.clip(jnp.exp(jax.random.uniform(streams_of[5], (ORDER, CH), jnp.float32, math.log(0.1), math.log(120.0))), 0.1, 120.0),
        "residue": normal_values(streams_of[6], (ORDER, CH), 0.25, 2.5, (), jnp.float32),
        "skip_gain": jnp.clip(jax.random.uniform(streams_of[7], (CH,), jnp.float32, 0.5, 1.5), 0.5, 1.5),
        "out_grad": normal_values(streams_of[8], (ROWS, SEQ, CH), 1.0, 6.0, ((0, 8), (1, 32))),
    }


def delayed(values, shift_by):
    if shift_by == 0:
        return values
    head = jnp.zeros((shift_by,) + values.shape[1:], values.dtype)
    return jnp.concatenate([head, values[:-shift_by]], axis=0)

def advanced(values, shift_by):
    if shift_by == 0:
        return values
    tail = jnp.zeros((shift_by,) + values.shape[1:], values.dtype)
    return jnp.concatenate([values[shift_by:], tail], axis=0)

def one_row(query_row, key_row, value_row, grad_row, offsets, short_taps, rate_scale, residue, skip_gain):
    lam_log = -rate_scale / SEQ
    decay_step = jnp.exp(lam_log)
    norm_factor = jnp.sqrt(-jnp.expm1(2.0 * lam_log))
    mode_coef = residue * norm_factor
    tap_count = short_taps.shape[1]
    sources = [query_row.astype(jnp.float32), key_row.astype(jnp.float32), value_row.astype(jnp.float32)]
    filtered = []
    for branch_index in range(3):
        summed = jnp.zeros_like(sources[branch_index])
        for tap_index in range(tap_count):
            inside_doc = (offsets >= tap_index)[:, None]
            summed = summed + short_taps[branch_index, tap_index] * jnp.where(inside_doc, delayed(sources[branch_index], tap_index), 0.0)
        filtered.append(summed)
    query_short, key_short, value_short = filtered
    mixed = key_short * value_short
    grad_in = grad_row.astype(jnp.float32)
    z_grad = grad_in * query_short
    continues = (offsets > 0).astype(jnp.float32)

    def forward_step(carry, inputs):
        modal_state, res_accum = carry
        mixed_now, grad_now, cont_now = inputs
        modal_state = decay_step * cont_now * modal_state + mixed_now[None, :]
        res_accum = res_accum + grad_now[None, :] * modal_state
        return ((modal_state, res_accum), lax.optimization_barrier(jnp.sum(mode_coef * modal_state, axis=0)))
    zero_state = jnp.zeros(rate_scale.shape, jnp.float32)
    (_, res_accum), long_out = lax.scan(forward_step, (zero_state, zero_state), (mixed, z_grad, continues))
    z_full = long_out + skip_gain * mixed
    mixed_out = (query_short * z_full).astype(jnp.bfloat16)
    cont_next = jnp.concatenate([continues[1:], jnp.zeros((1,), jnp.float32)])

    def backward_step(carried, inputs):
        grad_now, cont_now = inputs
        carried = grad_now[None, :] + decay_step * cont_now * carried
        return (carried, lax.optimization_barrier(jnp.sum(mode_coef * carried, axis=0)))
    _, long_back = lax.scan(backward_step, zero_state, (z_grad, cont_next), reverse=True)
    mixed_grad = long_back + skip_gain * z_grad
    short_grads = [grad_in * z_full, mixed_grad * value_short, mixed_grad * key_short]
    input_grads = []
    tap_terms = []
    for branch_index in range(3):
        branch_grad = short_grads[branch_index]
        summed = jnp.zeros_like(branch_grad)
        per_tap = []
        for tap_index in range(tap_count):
            masked = jnp.where((offsets >= tap_index)[:, None], branch_grad, 0.0)
            summed = summed + short_taps[branch_index, tap_index] * advanced(masked, tap_index)
            per_tap.append(lax.optimization_barrier(jnp.sum(masked * delayed(sources[branch_index], tap_index), axis=0)))
        input_grads.append(summed.astype(jnp.bfloat16))
        tap_terms.append(jnp.stack(per_tap))
    skip_term = lax.optimization_barrier(jnp.sum(z_grad * mixed, axis=0))
    return (mixed_out, input_grads[0], input_grads[1], input_grads[2], jnp.stack(tap_terms), skip_term, norm_factor * res_accum)

def reference(query_proj, key_proj, value_proj, doc_offset, short_taps, rate_scale, residue, skip_gain, out_grad):

    def per_row(pieces):
        return one_row(pieces[0], pieces[1], pieces[2], pieces[3], pieces[4], short_taps, rate_scale, residue, skip_gain)
    results = lax.map(per_row, (query_proj, key_proj, value_proj, out_grad, doc_offset))
    scale = 1.0 / math.sqrt(ROWS * SEQ)
    taps_grad = lax.optimization_barrier(jnp.sum(results[4], axis=0)) * scale
    skip_grad = lax.optimization_barrier(jnp.sum(results[5], axis=0)) * scale
    residue_grad = lax.optimization_barrier(jnp.sum(results[6], axis=0)) * scale
    return (results[0], results[1], results[2], results[3], taps_grad, skip_grad, residue_grad)
```

```python
import math

import jax
import jax.numpy as jnp
from jax import lax
from jax.sharding import PartitionSpec as P


def from_behind(block, axis, distance):
    devices = range(lax.axis_size(axis))
    route = [(i - distance, i) for i in devices if i - distance in devices]
    return lax.ppermute(block, axis, route)


def device_scan(flags, values, step_log, direction):
    count = lax.axis_size("ctx")
    gates = flags[:, None, None]
    sums = values
    distance = 1
    while distance < count:
        route = [(i, i + distance * direction) for i in range(count) if 0 <= i + distance * direction < count]
        got_gates, got_sums = lax.ppermute((gates, sums), "ctx", route)
        sums = sums + gates * jnp.exp(distance * step_log) * got_sums
        gates = gates * got_gates
        distance *= 2
    route = [(i, i + direction) for i in range(count) if 0 <= i + direction < count]
    return lax.ppermute(sums, "ctx", route)


def butterfly_sum(value, axes):
    for axis in axes:
        count = lax.axis_size(axis)
        if count & (count - 1):
            value = lax.psum(value, axis)
            continue
        step = 1
        while step < count:
            value = value + lax.ppermute(value, axis, [(i, i ^ step) for i in range(count)])
            step *= 2
    return value


def shards(
    query_proj,
    key_proj,
    value_proj,
    doc_offset,
    short_taps,
    rate_scale,
    residue,
    skip_gain,
    out_grad,
):
    row_count, tok_len, channels = query_proj.shape
    ctx_count = lax.axis_size("ctx")
    seq_len = tok_len * ctx_count
    total_tokens = row_count * lax.axis_size("dp") * seq_len
    ctx_index = lax.axis_index("ctx")
    tap_count = short_taps.shape[1]
    rim_len = tap_count - 1
    block_len = math.gcd(tok_len, 16)
    sub_count = tok_len // block_len
    rims = from_behind(
        (
            query_proj[:, tok_len - rim_len :, :],
            key_proj[:, tok_len - rim_len :, :],
            value_proj[:, tok_len - rim_len :, :],
        ),
        "ctx",
        1,
    )
    sources = (query_proj, key_proj, value_proj)
    extended = jnp.stack(
        [
            jnp.concatenate([rims[branch_index], sources[branch_index]], axis=1)
            for branch_index in range(3)
        ],
        axis=0,
    )
    tap_masks = [(doc_offset >= tap_index)[None, :, :, None] for tap_index in range(tap_count)]

    def window(tap_index):
        piece = extended[:, :, rim_len - tap_index : rim_len - tap_index + tok_len, :].astype(
            jnp.float32
        )
        return jnp.where(tap_masks[tap_index], piece, 0.0)

    shorts = jnp.zeros((3, row_count, tok_len, channels), jnp.float32)
    for tap_index in range(tap_count):
        shorts = shorts + short_taps[:, tap_index][:, None, None, :] * window(tap_index)
    query_short = shorts[0]
    key_short = shorts[1]
    value_short = shorts[2]
    lam_log = -rate_scale / seq_len
    decay_step = jnp.exp(lam_log)
    norm_factor = jnp.sqrt(-jnp.expm1(2.0 * lam_log))
    mode_coef = residue * norm_factor
    slot_index = jnp.arange(block_len, dtype=jnp.int32)
    slot_float = slot_index.astype(jnp.float32)
    pow_zero = jnp.exp(slot_float[:, None, None] * lam_log[None, :, :])
    pow_one = pow_zero * decay_step[None]
    pow_end = pow_zero[::-1]
    pow_back = pow_one[::-1]
    filter_taps = jnp.sum(mode_coef[None] * pow_zero, axis=1)
    decay_block = jnp.exp(block_len * lam_log)
    offsets = doc_offset.reshape(row_count, sub_count, block_len)
    valid_in = (offsets > slot_index[None, None, :]).astype(jnp.float32)[..., None]
    last_doc = (slot_index[None, None, :] >= block_len - 1 - offsets[:, :, -1:]).astype(
        jnp.float32
    )[..., None]
    pass_sub = (offsets[:, :, -1] >= block_len).astype(jnp.float32)
    pass_dev = (doc_offset[:, -1] >= tok_len).astype(jnp.float32)
    zero_state = jnp.zeros((row_count,) + rate_scale.shape, jnp.float32)
    lag_masks = [(offsets >= lag)[..., None] for lag in range(block_len)]

    def intra_backward(grads):
        total = jnp.zeros_like(grads)
        for lag in range(block_len):
            masked = jnp.where(lag_masks[lag], grads, 0.0)
            padded = jnp.pad(masked, ((0, 0), (0, 0), (0, block_len), (0, 0)))
            total = total + filter_taps[lag] * padded[:, :, lag : lag + block_len, :]
        return total

    def sweep(initial, terms, reverse_flag):
        carried = initial
        visited = [None] * sub_count
        order = range(sub_count - 1, -1, -1) if reverse_flag else range(sub_count)
        for sub_index in order:
            visited[sub_index] = carried
            passed = pass_sub[:, sub_index][:, None, None]
            carried = terms[sub_index] + decay_block * passed * carried
        return carried, jnp.stack(visited)

    mixed = key_short * value_short
    mixed_blocks = mixed.reshape(row_count, sub_count, block_len, channels)
    intra_padded = jnp.pad(mixed_blocks, ((0, 0), (0, 0), (block_len, 0), (0, 0)))
    total = jnp.zeros_like(mixed_blocks)
    for intra_lag in range(block_len):
        shifted = intra_padded[:, :, block_len - intra_lag : 2 * block_len - intra_lag, :]
        total = total + filter_taps[intra_lag] * jnp.where(lag_masks[intra_lag], shifted, 0.0)
    sigma = jnp.swapaxes(
        jnp.sum(pow_end[None, None] * (mixed_blocks * last_doc)[:, :, :, None, :], axis=2), 0, 1
    )
    block_sum, _ = sweep(zero_state, sigma, False)
    states = device_scan(pass_dev, block_sum, tok_len * lam_log, 1)
    _, enters = sweep(states, sigma, False)
    cross = valid_in * jnp.sum(
        (mode_coef[None] * pow_one)[None, None] * jnp.swapaxes(enters, 0, 1)[:, :, None], axis=3
    )
    long_out = (total + cross).reshape(row_count, tok_len, channels)
    z_full = long_out + skip_gain * mixed
    mixed_out = (query_short * z_full).astype(jnp.bfloat16)
    grad_in = out_grad.astype(jnp.float32)
    z_grad = grad_in * query_short
    query_short_grad = grad_in * z_full
    grad_blocks = z_grad.reshape(row_count, sub_count, block_len, channels)
    inner_back = intra_backward(grad_blocks)
    gamma = jnp.swapaxes(
        jnp.sum(pow_zero[None, None] * (grad_blocks * valid_in)[:, :, :, None, :], axis=2), 0, 1
    )
    block_adj, _ = sweep(zero_state, gamma, True)
    adj_in = device_scan(pass_dev, block_adj, tok_len * lam_log, -1)
    _, exits = sweep(adj_in, gamma, True)
    cross_back = last_doc * jnp.sum(
        (mode_coef[None] * pow_back)[None, None] * jnp.swapaxes(exits, 0, 1)[:, :, None], axis=3
    )
    mixed_grad = (inner_back + cross_back).reshape(
        row_count, tok_len, channels
    ) + skip_gain * z_grad
    key_short_grad = mixed_grad * value_short
    value_short_grad = mixed_grad * key_short
    padded_mixed = jnp.pad(mixed_blocks, ((0, 0), (0, 0), (block_len, 0), (0, 0)))
    lag_sums = jnp.stack(
        [
            jnp.sum(
                grad_blocks
                * jnp.where(
                    lag_masks[lag],
                    padded_mixed[:, :, block_len - lag : 2 * block_len - lag, :],
                    0.0,
                ),
                axis=(0, 1, 2),
            )
            for lag in range(block_len)
        ],
        axis=0,
    )
    residue_term = norm_factor * (
        jnp.sum(lag_sums[:, None, :] * pow_zero, axis=0)
        + jnp.sum(decay_step[None, None] * gamma * enters, axis=(0, 1))
    )
    skip_term = jnp.sum(z_grad * mixed, axis=(0, 1))
    short_grads = jnp.stack([query_short_grad, key_short_grad, value_short_grad], axis=0)
    spread = jnp.zeros((3, row_count, tok_len + rim_len, channels), jnp.float32)
    tap_terms = []
    for tap_index in range(tap_count):
        masked = jnp.where(tap_masks[tap_index], short_grads, 0.0)
        padded = jnp.pad(masked, ((0, 0), (0, 0), (rim_len, rim_len), (0, 0)))
        spread = (
            spread
            + short_taps[:, tap_index][:, None, None, :]
            * padded[:, :, tap_index : tap_index + tok_len + rim_len, :]
        )
        tap_terms.append(jnp.sum(window(tap_index) * short_grads, axis=(1, 2)))
    heads = spread[:, :, :rim_len, :]
    owns = spread[:, :, rim_len:, :]
    incoming = from_behind((heads[0], heads[1], heads[2]), "ctx", -1)
    input_grads = [
        (
            owns[branch_index]
            + jnp.pad(incoming[branch_index], ((0, 0), (tok_len - rim_len, 0), (0, 0)))
        ).astype(jnp.bfloat16)
        for branch_index in range(3)
    ]
    tap_stack = jnp.stack(tap_terms, axis=1)
    flat = jnp.concatenate([tap_stack.reshape(-1), skip_term, residue_term.reshape(-1)])
    flat = butterfly_sum(flat, ("ctx", "dp"))
    taps_sum = flat[: tap_stack.size].reshape(tap_stack.shape)
    skip_sum = flat[tap_stack.size : tap_stack.size + skip_term.size]
    residue_sum = flat[tap_stack.size + skip_term.size :].reshape(residue_term.shape)
    scale = 1.0 / math.sqrt(total_tokens)
    return (
        mixed_out,
        input_grads[0],
        input_grads[1],
        input_grads[2],
        taps_sum * scale,
        skip_sum * scale,
        residue_sum * scale,
    )


def solution(mesh):
    in_specs = (
        P("dp", "ctx", None),
        P("dp", "ctx", None),
        P("dp", "ctx", None),
        P("dp", "ctx"),
        P(),
        P(),
        P(),
        P(),
        P("dp", "ctx", None),
    )
    out_specs = (
        P("dp", "ctx", None),
        P("dp", "ctx", None),
        P("dp", "ctx", None),
        P("dp", "ctx", None),
        P(),
        P(),
        P(),
    )
    return jax.shard_map(shards, mesh=mesh, in_specs=in_specs, out_specs=out_specs, check_vma=False)
```

```python
import math

import jax
import jax.numpy as jnp
from jax import lax
from jax.sharding import PartitionSpec as P


def from_behind(block, axis, distance):
    devices = range(lax.axis_size(axis))
    route = [(i - distance, i) for i in devices if i - distance in devices]
    return lax.ppermute(block, axis, route)


def device_scan(ends, values, step_log, direction, tok_len):
    count = lax.axis_size("ctx")
    sums = values
    distance = 1
    while distance < count:
        route = [(i, i + distance * direction) for i in range(count) if 0 <= i + distance * direction < count]
        gate = (ends >= distance * tok_len) if direction > 0 else (ends > distance * tok_len)
        gate = gate.astype(jnp.float32)[:, None, None]
        if direction > 0:
            sums = sums + gate * jnp.exp(distance * step_log) * lax.ppermute(sums, "ctx", route)
        else:
            sums = sums + jnp.exp(distance * step_log) * lax.ppermute(gate * sums, "ctx", route)
        distance *= 2
    route = [(i, i + direction) for i in range(count) if 0 <= i + direction < count]
    return lax.ppermute(sums, "ctx", route)


def butterfly_sum(value, axes):
    for axis in axes:
        count = lax.axis_size(axis)
        if count & (count - 1):
            value = lax.psum(value, axis)
            continue
        step = 1
        while step < count:
            value = value + lax.ppermute(value, axis, [(i, i ^ step) for i in range(count)])
            step *= 2
    return value


def spread_sum(value, scatter_axis, other_axes):
    count = lax.axis_size(scatter_axis)
    if count & (count - 1) or value.shape[0] % count:
        return butterfly_sum(value, (scatter_axis,) + tuple(other_axes))
    index = lax.axis_index(scatter_axis)
    lanes = 128 if (value.shape[0] // count) % 128 == 0 else 1
    blocks = value.reshape(count, -1, lanes)
    step = count // 2
    while step >= 1:
        half = blocks.shape[0] // 2
        low = (index // step) % 2 == 0
        keep = jnp.where(low, blocks[:half], blocks[half:])
        send = jnp.where(low, blocks[half:], blocks[:half])
        blocks = keep + lax.ppermute(send, scatter_axis, [(i, i ^ step) for i in range(count)])
        step //= 2
    blocks = butterfly_sum(blocks, other_axes)
    step = 1
    while step < count:
        got = lax.ppermute(blocks, scatter_axis, [(i, i ^ step) for i in range(count)])
        low = (index // step) % 2 == 0
        blocks = jnp.where(low, jnp.concatenate([blocks, got]), jnp.concatenate([got, blocks]))
        step *= 2
    return blocks.reshape(-1)


def shards(
    query_proj,
    key_proj,
    value_proj,
    doc_offset,
    short_taps,
    rate_scale,
    residue,
    skip_gain,
    out_grad,
):
    row_count, tok_len, channels = query_proj.shape
    ctx_count = lax.axis_size("ctx")
    seq_len = tok_len * ctx_count
    total_tokens = row_count * lax.axis_size("dp") * seq_len
    ctx_index = lax.axis_index("ctx")
    tap_count = short_taps.shape[1]
    rim_len = tap_count - 1
    block_len = math.gcd(tok_len, 16)
    sub_count = tok_len // block_len
    rims = from_behind(
        (
            query_proj[:, tok_len - rim_len :, :],
            key_proj[:, tok_len - rim_len :, :],
            value_proj[:, tok_len - rim_len :, :],
        ),
        "ctx",
        1,
    )
    sources = (query_proj, key_proj, value_proj)
    extended = jnp.stack(
        [
            jnp.concatenate([rims[branch_index], sources[branch_index]], axis=1)
            for branch_index in range(3)
        ],
        axis=0,
    )
    tap_masks = [(doc_offset >= tap_index)[None, :, :, None] for tap_index in range(tap_count)]

    def window(tap_index):
        piece = extended[:, :, rim_len - tap_index : rim_len - tap_index + tok_len, :].astype(
            jnp.float32
        )
        return jnp.where(tap_masks[tap_index], piece, 0.0)

    shorts = jnp.zeros((3, row_count, tok_len, channels), jnp.float32)
    for tap_index in range(tap_count):
        shorts = shorts + short_taps[:, tap_index][:, None, None, :] * window(tap_index)
    query_short = shorts[0]
    key_short = shorts[1]
    value_short = shorts[2]
    lam_log = -rate_scale / seq_len
    decay_step = jnp.exp(lam_log)
    norm_factor = jnp.sqrt(-jnp.expm1(2.0 * lam_log))
    mode_coef = residue * norm_factor
    slot_index = jnp.arange(block_len, dtype=jnp.int32)
    slot_float = slot_index.astype(jnp.float32)
    pow_zero = jnp.exp(slot_float[:, None, None] * lam_log[None, :, :])
    pow_one = pow_zero * decay_step[None]
    pow_end = pow_zero[::-1]
    pow_back = pow_one[::-1]
    filter_taps = jnp.sum(mode_coef[None] * pow_zero, axis=1)
    decay_block = jnp.exp(block_len * lam_log)
    offsets = doc_offset.reshape(row_count, sub_count, block_len)
    valid_in = (offsets > slot_index[None, None, :]).astype(jnp.float32)[..., None]
    last_doc = (slot_index[None, None, :] >= block_len - 1 - offsets[:, :, -1:]).astype(
        jnp.float32
    )[..., None]
    pass_sub = (offsets[:, :, -1] >= block_len).astype(jnp.float32)
    pass_dev = (doc_offset[:, -1] >= tok_len).astype(jnp.float32)
    zero_state = jnp.zeros((row_count,) + rate_scale.shape, jnp.float32)
    lag_masks = [(offsets >= lag)[..., None] for lag in range(block_len)]

    def intra_backward(grads):
        total = jnp.zeros_like(grads)
        for lag in range(block_len):
            masked = jnp.where(lag_masks[lag], grads, 0.0)
            padded = jnp.pad(masked, ((0, 0), (0, 0), (0, block_len), (0, 0)))
            total = total + filter_taps[lag] * padded[:, :, lag : lag + block_len, :]
        return total

    def sweep(initial, terms, reverse_flag):
        carried = initial
        visited = [None] * sub_count
        order = range(sub_count - 1, -1, -1) if reverse_flag else range(sub_count)
        for sub_index in order:
            visited[sub_index] = carried
            passed = pass_sub[:, sub_index][:, None, None]
            carried = terms[sub_index] + decay_block * passed * carried
        return carried, jnp.stack(visited)

    mixed = key_short * value_short
    mixed_blocks = mixed.reshape(row_count, sub_count, block_len, channels)
    intra_padded = jnp.pad(mixed_blocks, ((0, 0), (0, 0), (block_len, 0), (0, 0)))
    total = jnp.zeros_like(mixed_blocks)
    for intra_lag in range(block_len):
        shifted = intra_padded[:, :, block_len - intra_lag : 2 * block_len - intra_lag, :]
        total = total + filter_taps[intra_lag] * jnp.where(lag_masks[intra_lag], shifted, 0.0)
    sigma = jnp.swapaxes(
        jnp.sum(pow_end[None, None] * (mixed_blocks * last_doc)[:, :, :, None, :], axis=2), 0, 1
    )
    block_sum, _ = sweep(zero_state, sigma, False)
    states = device_scan(doc_offset[:, -1], block_sum, tok_len * lam_log, 1, tok_len)
    _, enters = sweep(states, sigma, False)
    cross = valid_in * jnp.sum(
        (mode_coef[None] * pow_one)[None, None] * jnp.swapaxes(enters, 0, 1)[:, :, None], axis=3
    )
    long_out = (total + cross).reshape(row_count, tok_len, channels)
    z_full = long_out + skip_gain * mixed
    mixed_out = (query_short * z_full).astype(jnp.bfloat16)
    grad_in = out_grad.astype(jnp.float32)
    z_grad = grad_in * query_short
    query_short_grad = grad_in * z_full
    grad_blocks = z_grad.reshape(row_count, sub_count, block_len, channels)
    inner_back = intra_backward(grad_blocks)
    gamma = jnp.swapaxes(
        jnp.sum(pow_zero[None, None] * (grad_blocks * valid_in)[:, :, :, None, :], axis=2), 0, 1
    )
    block_adj, _ = sweep(zero_state, gamma, True)
    adj_in = device_scan(doc_offset[:, 0], block_adj, tok_len * lam_log, -1, tok_len)
    _, exits = sweep(adj_in, gamma, True)
    cross_back = last_doc * jnp.sum(
        (mode_coef[None] * pow_back)[None, None] * jnp.swapaxes(exits, 0, 1)[:, :, None], axis=3
    )
    mixed_grad = (inner_back + cross_back).reshape(
        row_count, tok_len, channels
    ) + skip_gain * z_grad
    key_short_grad = mixed_grad * value_short
    value_short_grad = mixed_grad * key_short
    padded_mixed = jnp.pad(mixed_blocks, ((0, 0), (0, 0), (block_len, 0), (0, 0)))
    lag_sums = jnp.stack(
        [
            jnp.sum(
                grad_blocks
                * jnp.where(
                    lag_masks[lag],
                    padded_mixed[:, :, block_len - lag : 2 * block_len - lag, :],
                    0.0,
                ),
                axis=(0, 1, 2),
            )
            for lag in range(block_len)
        ],
        axis=0,
    )
    residue_term = norm_factor * (
        jnp.sum(lag_sums[:, None, :] * pow_zero, axis=0)
        + jnp.sum(decay_step[None, None] * gamma * enters, axis=(0, 1))
    )
    skip_term = jnp.sum(z_grad * mixed, axis=(0, 1))
    short_grads = jnp.stack([query_short_grad, key_short_grad, value_short_grad], axis=0)
    spread = jnp.zeros((3, row_count, tok_len + rim_len, channels), jnp.float32)
    tap_terms = []
    for tap_index in range(tap_count):
        masked = jnp.where(tap_masks[tap_index], short_grads, 0.0)
        padded = jnp.pad(masked, ((0, 0), (0, 0), (rim_len, rim_len), (0, 0)))
        spread = (
            spread
            + short_taps[:, tap_index][:, None, None, :]
            * padded[:, :, tap_index : tap_index + tok_len + rim_len, :]
        )
        tap_terms.append(jnp.sum(window(tap_index) * short_grads, axis=(1, 2)))
    heads = spread[:, :, :rim_len, :]
    owns = spread[:, :, rim_len:, :]
    incoming = from_behind((heads[0], heads[1], heads[2]), "ctx", -1)
    input_grads = [
        (
            owns[branch_index]
            + jnp.pad(incoming[branch_index], ((0, 0), (tok_len - rim_len, 0), (0, 0)))
        ).astype(jnp.bfloat16)
        for branch_index in range(3)
    ]
    tap_stack = jnp.stack(tap_terms, axis=1)
    flat = jnp.concatenate([tap_stack.reshape(-1), skip_term, residue_term.reshape(-1)])
    flat = spread_sum(flat, "ctx", ("dp",))
    taps_sum = flat[: tap_stack.size].reshape(tap_stack.shape)
    skip_sum = flat[tap_stack.size : tap_stack.size + skip_term.size]
    residue_sum = flat[tap_stack.size + skip_term.size :].reshape(residue_term.shape)
    scale = 1.0 / math.sqrt(total_tokens)
    return (
        mixed_out,
        input_grads[0],
        input_grads[1],
        input_grads[2],
        taps_sum * scale,
        skip_sum * scale,
        residue_sum * scale,
    )


def solution(mesh):
    in_specs = (
        P("dp", "ctx", None),
        P("dp", "ctx", None),
        P("dp", "ctx", None),
        P("dp", "ctx"),
        P(),
        P(),
        P(),
        P(),
        P("dp", "ctx", None),
    )
    out_specs = (
        P("dp", "ctx", None),
        P("dp", "ctx", None),
        P("dp", "ctx", None),
        P("dp", "ctx", None),
        P(),
        P(),
        P(),
    )
    return jax.shard_map(shards, mesh=mesh, in_specs=in_specs, out_specs=out_specs, check_vma=False)
```

```python
import math

import jax
import jax.numpy as jnp
from jax import lax
from jax.sharding import PartitionSpec as P


def from_behind(block, axis, distance):
    devices = range(lax.axis_size(axis))
    route = [(i - distance, i) for i in devices if i - distance in devices]
    return lax.ppermute(block, axis, route)


def device_scan(ends, values, step_log, direction, tok_len):
    count = lax.axis_size("ctx")
    sums = values
    distance = 1
    while distance < count:
        route = [(i, i + distance * direction) for i in range(count) if 0 <= i + distance * direction < count]
        gate = (ends >= distance * tok_len) if direction > 0 else (ends > distance * tok_len)
        gate = gate.astype(jnp.float32)[:, None, None]
        if direction > 0:
            sums = sums + gate * jnp.exp(distance * step_log) * lax.ppermute(sums, "ctx", route)
        else:
            sums = sums + jnp.exp(distance * step_log) * lax.ppermute(gate * sums, "ctx", route)
        distance *= 2
    route = [(i, i + direction) for i in range(count) if 0 <= i + direction < count]
    return lax.ppermute(sums, "ctx", route)


def butterfly_sum(value, axes):
    for axis in axes:
        count = lax.axis_size(axis)
        if count & (count - 1):
            value = lax.psum(value, axis)
            continue
        step = 1
        while step < count:
            value = value + lax.ppermute(value, axis, [(i, i ^ step) for i in range(count)])
            step *= 2
    return value


def spread_sum(value, scatter_axis, other_axes):
    count = lax.axis_size(scatter_axis)
    if count & (count - 1) or value.shape[0] % count:
        return butterfly_sum(value, (scatter_axis,) + tuple(other_axes))
    index = lax.axis_index(scatter_axis)
    lanes = 128 if (value.shape[0] // count) % 128 == 0 else 1
    blocks = value.reshape(count, -1, lanes)
    steps = [1 << bit for bit in range(count.bit_length() - 1)]
    steps = [s for s in steps if s in (1, 4)] + [s for s in steps if s not in (1, 4)]
    for step in steps:
        half = blocks.shape[0] // 2
        low = (index // step) % 2 == 0
        keep = jnp.where(low, blocks[:half], blocks[half:])
        send = jnp.where(low, blocks[half:], blocks[:half])
        blocks = keep + lax.ppermute(send, scatter_axis, [(i, i ^ step) for i in range(count)])
    blocks = butterfly_sum(blocks, other_axes)
    for step in reversed(steps):
        got = lax.ppermute(blocks, scatter_axis, [(i, i ^ step) for i in range(count)])
        low = (index // step) % 2 == 0
        blocks = jnp.where(low, jnp.concatenate([blocks, got]), jnp.concatenate([got, blocks]))
    return blocks.reshape(-1)


def shards(
    query_proj,
    key_proj,
    value_proj,
    doc_offset,
    short_taps,
    rate_scale,
    residue,
    skip_gain,
    out_grad,
):
    row_count, tok_len, channels = query_proj.shape
    ctx_count = lax.axis_size("ctx")
    seq_len = tok_len * ctx_count
    total_tokens = row_count * lax.axis_size("dp") * seq_len
    ctx_index = lax.axis_index("ctx")
    tap_count = short_taps.shape[1]
    rim_len = tap_count - 1
    block_len = math.gcd(tok_len, 16)
    sub_count = tok_len // block_len
    rims = from_behind(
        (
            query_proj[:, tok_len - rim_len :, :],
            key_proj[:, tok_len - rim_len :, :],
            value_proj[:, tok_len - rim_len :, :],
        ),
        "ctx",
        1,
    )
    sources = (query_proj, key_proj, value_proj)
    extended = jnp.stack(
        [
            jnp.concatenate([rims[branch_index], sources[branch_index]], axis=1)
            for branch_index in range(3)
        ],
        axis=0,
    )
    tap_masks = [(doc_offset >= tap_index)[None, :, :, None] for tap_index in range(tap_count)]

    def window(tap_index):
        piece = extended[:, :, rim_len - tap_index : rim_len - tap_index + tok_len, :].astype(
            jnp.float32
        )
        return jnp.where(tap_masks[tap_index], piece, 0.0)

    shorts = jnp.zeros((3, row_count, tok_len, channels), jnp.float32)
    for tap_index in range(tap_count):
        shorts = shorts + short_taps[:, tap_index][:, None, None, :] * window(tap_index)
    query_short = shorts[0]
    key_short = shorts[1]
    value_short = shorts[2]
    lam_log = -rate_scale / seq_len
    decay_step = jnp.exp(lam_log)
    norm_factor = jnp.sqrt(-jnp.expm1(2.0 * lam_log))
    mode_coef = residue * norm_factor
    slot_index = jnp.arange(block_len, dtype=jnp.int32)
    slot_float = slot_index.astype(jnp.float32)
    pow_zero = jnp.exp(slot_float[:, None, None] * lam_log[None, :, :])
    pow_one = pow_zero * decay_step[None]
    pow_end = pow_zero[::-1]
    pow_back = pow_one[::-1]
    filter_taps = jnp.sum(mode_coef[None] * pow_zero, axis=1)
    decay_block = jnp.exp(block_len * lam_log)
    offsets = doc_offset.reshape(row_count, sub_count, block_len)
    valid_in = (offsets > slot_index[None, None, :]).astype(jnp.float32)[..., None]
    last_doc = (slot_index[None, None, :] >= block_len - 1 - offsets[:, :, -1:]).astype(
        jnp.float32
    )[..., None]
    pass_sub = (offsets[:, :, -1] >= block_len).astype(jnp.float32)
    pass_dev = (doc_offset[:, -1] >= tok_len).astype(jnp.float32)
    zero_state = jnp.zeros((row_count,) + rate_scale.shape, jnp.float32)
    lag_masks = [(offsets >= lag)[..., None] for lag in range(block_len)]

    def intra_backward(grads):
        total = jnp.zeros_like(grads)
        for lag in range(block_len):
            masked = jnp.where(lag_masks[lag], grads, 0.0)
            padded = jnp.pad(masked, ((0, 0), (0, 0), (0, block_len), (0, 0)))
            total = total + filter_taps[lag] * padded[:, :, lag : lag + block_len, :]
        return total

    def sweep(initial, terms, reverse_flag):
        carried = initial
        visited = [None] * sub_count
        order = range(sub_count - 1, -1, -1) if reverse_flag else range(sub_count)
        for sub_index in order:
            visited[sub_index] = carried
            passed = pass_sub[:, sub_index][:, None, None]
            carried = terms[sub_index] + decay_block * passed * carried
        return carried, jnp.stack(visited)

    mixed = key_short * value_short
    mixed_blocks = mixed.reshape(row_count, sub_count, block_len, channels)
    intra_padded = jnp.pad(mixed_blocks, ((0, 0), (0, 0), (block_len, 0), (0, 0)))
    total = jnp.zeros_like(mixed_blocks)
    for intra_lag in range(block_len):
        shifted = intra_padded[:, :, block_len - intra_lag : 2 * block_len - intra_lag, :]
        total = total + filter_taps[intra_lag] * jnp.where(lag_masks[intra_lag], shifted, 0.0)
    sigma = jnp.swapaxes(
        jnp.sum(pow_end[None, None] * (mixed_blocks * last_doc)[:, :, :, None, :], axis=2), 0, 1
    )
    block_sum, _ = sweep(zero_state, sigma, False)
    states = device_scan(doc_offset[:, -1], block_sum, tok_len * lam_log, 1, tok_len)
    _, enters = sweep(states, sigma, False)
    cross = valid_in * jnp.sum(
        (mode_coef[None] * pow_one)[None, None] * jnp.swapaxes(enters, 0, 1)[:, :, None], axis=3
    )
    long_out = (total + cross).reshape(row_count, tok_len, channels)
    z_full = long_out + skip_gain * mixed
    mixed_out = (query_short * z_full).astype(jnp.bfloat16)
    grad_in = out_grad.astype(jnp.float32)
    z_grad = grad_in * query_short
    query_short_grad = grad_in * z_full
    grad_blocks = z_grad.reshape(row_count, sub_count, block_len, channels)
    inner_back = intra_backward(grad_blocks)
    gamma = jnp.swapaxes(
        jnp.sum(pow_zero[None, None] * (grad_blocks * valid_in)[:, :, :, None, :], axis=2), 0, 1
    )
    block_adj, _ = sweep(zero_state, gamma, True)
    adj_in = device_scan(doc_offset[:, 0], block_adj, tok_len * lam_log, -1, tok_len)
    _, exits = sweep(adj_in, gamma, True)
    cross_back = last_doc * jnp.sum(
        (mode_coef[None] * pow_back)[None, None] * jnp.swapaxes(exits, 0, 1)[:, :, None], axis=3
    )
    mixed_grad = (inner_back + cross_back).reshape(
        row_count, tok_len, channels
    ) + skip_gain * z_grad
    key_short_grad = mixed_grad * value_short
    value_short_grad = mixed_grad * key_short
    padded_mixed = jnp.pad(mixed_blocks, ((0, 0), (0, 0), (block_len, 0), (0, 0)))
    lag_sums = jnp.stack(
        [
            jnp.sum(
                grad_blocks
                * jnp.where(
                    lag_masks[lag],
                    padded_mixed[:, :, block_len - lag : 2 * block_len - lag, :],
                    0.0,
                ),
                axis=(0, 1, 2),
            )
            for lag in range(block_len)
        ],
        axis=0,
    )
    residue_term = norm_factor * (
        jnp.sum(lag_sums[:, None, :] * pow_zero, axis=0)
        + jnp.sum(decay_step[None, None] * gamma * enters, axis=(0, 1))
    )
    skip_term = jnp.sum(z_grad * mixed, axis=(0, 1))
    short_grads = jnp.stack([query_short_grad, key_short_grad, value_short_grad], axis=0)
    spread = jnp.zeros((3, row_count, tok_len + rim_len, channels), jnp.float32)
    tap_terms = []
    for tap_index in range(tap_count):
        masked = jnp.where(tap_masks[tap_index], short_grads, 0.0)
        padded = jnp.pad(masked, ((0, 0), (0, 0), (rim_len, rim_len), (0, 0)))
        spread = (
            spread
            + short_taps[:, tap_index][:, None, None, :]
            * padded[:, :, tap_index : tap_index + tok_len + rim_len, :]
        )
        tap_terms.append(jnp.sum(window(tap_index) * short_grads, axis=(1, 2)))
    heads = spread[:, :, :rim_len, :]
    owns = spread[:, :, rim_len:, :]
    incoming = from_behind((heads[0], heads[1], heads[2]), "ctx", -1)
    input_grads = [
        (
            owns[branch_index]
            + jnp.pad(incoming[branch_index], ((0, 0), (tok_len - rim_len, 0), (0, 0)))
        ).astype(jnp.bfloat16)
        for branch_index in range(3)
    ]
    tap_stack = jnp.stack(tap_terms, axis=1)
    flat = jnp.concatenate([tap_stack.reshape(-1), skip_term, residue_term.reshape(-1)])
    flat = spread_sum(flat, "ctx", ("dp",))
    taps_sum = flat[: tap_stack.size].reshape(tap_stack.shape)
    skip_sum = flat[tap_stack.size : tap_stack.size + skip_term.size]
    residue_sum = flat[tap_stack.size + skip_term.size :].reshape(residue_term.shape)
    scale = 1.0 / math.sqrt(total_tokens)
    return (
        mixed_out,
        input_grads[0],
        input_grads[1],
        input_grads[2],
        taps_sum * scale,
        skip_sum * scale,
        residue_sum * scale,
    )


def solution(mesh):
    in_specs = (
        P("dp", "ctx", None),
        P("dp", "ctx", None),
        P("dp", "ctx", None),
        P("dp", "ctx"),
        P(),
        P(),
        P(),
        P(),
        P("dp", "ctx", None),
    )
    out_specs = (
        P("dp", "ctx", None),
        P("dp", "ctx", None),
        P("dp", "ctx", None),
        P("dp", "ctx", None),
        P(),
        P(),
        P(),
    )
    return jax.shard_map(shards, mesh=mesh, in_specs=in_specs, out_specs=out_specs, check_vma=False)
```

```python
import math

import jax
import jax.numpy as jnp
from jax import lax
from jax.sharding import PartitionSpec as P


def from_behind(block, axis, distance):
    devices = range(lax.axis_size(axis))
    route = [(i - distance, i) for i in devices if i - distance in devices]
    return lax.ppermute(block, axis, route)


def device_scan(ends, values, step_log, direction, tok_len):
    count = lax.axis_size("ctx")
    sums = values
    distance = 1
    while distance < count:
        route = [(i, i + distance * direction) for i in range(count) if 0 <= i + distance * direction < count]
        gate = (ends >= distance * tok_len) if direction > 0 else (ends > distance * tok_len)
        gate = gate.astype(jnp.float32)[:, None, None]
        if direction > 0:
            sums = sums + gate * jnp.exp(distance * step_log) * lax.ppermute(sums, "ctx", route)
        else:
            sums = sums + jnp.exp(distance * step_log) * lax.ppermute(gate * sums, "ctx", route)
        distance *= 2
    route = [(i, i + direction) for i in range(count) if 0 <= i + direction < count]
    return lax.ppermute(sums, "ctx", route)


def butterfly_sum(value, axes):
    for axis in axes:
        count = lax.axis_size(axis)
        if count & (count - 1):
            value = lax.psum(value, axis)
            continue
        step = 1
        while step < count:
            value = value + lax.ppermute(value, axis, [(i, i ^ step) for i in range(count)])
            step *= 2
    return value


def spread_sum(value, scatter_axis, other_axes):
    count = lax.axis_size(scatter_axis)
    if count & (count - 1) or value.shape[0] % count:
        return butterfly_sum(value, (scatter_axis,) + tuple(other_axes))
    index = lax.axis_index(scatter_axis)
    lanes = 128 if (value.shape[0] // count) % 128 == 0 else 1
    blocks = value.reshape(count, -1, lanes)
    steps = [1 << bit for bit in range(count.bit_length() - 1)]
    steps = [s for s in steps if s in (1, 4)] + [s for s in steps if s not in (1, 4)]
    for step in steps:
        half = blocks.shape[0] // 2
        low = (index // step) % 2 == 0
        keep = jnp.where(low, blocks[:half], blocks[half:])
        send = jnp.where(low, blocks[half:], blocks[:half])
        blocks = keep + lax.ppermute(send, scatter_axis, [(i, i ^ step) for i in range(count)])
    blocks = butterfly_sum(blocks, other_axes)
    for step in reversed(steps):
        got = lax.ppermute(blocks, scatter_axis, [(i, i ^ step) for i in range(count)])
        low = (index // step) % 2 == 0
        blocks = jnp.where(low, jnp.concatenate([blocks, got]), jnp.concatenate([got, blocks]))
    return blocks.reshape(-1)


def shards(
    query_proj,
    key_proj,
    value_proj,
    doc_offset,
    short_taps,
    rate_scale,
    residue,
    skip_gain,
    out_grad,
):
    row_count, tok_len, channels = query_proj.shape
    ctx_count = lax.axis_size("ctx")
    seq_len = tok_len * ctx_count
    total_tokens = row_count * lax.axis_size("dp") * seq_len
    ctx_index = lax.axis_index("ctx")
    tap_count = short_taps.shape[1]
    rim_len = tap_count - 1
    block_len = math.gcd(tok_len, 16)
    sub_count = tok_len // block_len
    rims = from_behind(
        (
            query_proj[:, tok_len - rim_len :, :],
            key_proj[:, tok_len - rim_len :, :],
            value_proj[:, tok_len - rim_len :, :],
        ),
        "ctx",
        1,
    )
    sources = (query_proj, key_proj, value_proj)
    extended = jnp.stack(
        [
            jnp.concatenate([rims[branch_index], sources[branch_index]], axis=1)
            for branch_index in range(3)
        ],
        axis=0,
    )
    tap_masks = [(doc_offset >= tap_index)[None, :, :, None] for tap_index in range(tap_count)]

    def window(tap_index):
        piece = extended[:, :, rim_len - tap_index : rim_len - tap_index + tok_len, :].astype(
            jnp.float32
        )
        return jnp.where(tap_masks[tap_index], piece, 0.0)

    shorts = jnp.zeros((3, row_count, tok_len, channels), jnp.float32)
    for tap_index in range(tap_count):
        shorts = shorts + short_taps[:, tap_index][:, None, None, :] * window(tap_index)
    query_short = shorts[0]
    key_short = shorts[1]
    value_short = shorts[2]
    lam_log = -rate_scale / seq_len
    decay_step = jnp.exp(lam_log)
    norm_factor = jnp.sqrt(-jnp.expm1(2.0 * lam_log))
    mode_coef = residue * norm_factor
    slot_index = jnp.arange(block_len, dtype=jnp.int32)
    slot_float = slot_index.astype(jnp.float32)
    pow_zero = jnp.exp(slot_float[:, None, None] * lam_log[None, :, :])
    pow_one = pow_zero * decay_step[None]
    pow_end = pow_zero[::-1]
    pow_back = pow_one[::-1]
    filter_taps = jnp.sum(mode_coef[None] * pow_zero, axis=1)
    decay_block = jnp.exp(block_len * lam_log)
    offsets = doc_offset.reshape(row_count, sub_count, block_len)
    valid_in = (offsets > slot_index[None, None, :]).astype(jnp.float32)[..., None]
    last_doc = (slot_index[None, None, :] >= block_len - 1 - offsets[:, :, -1:]).astype(
        jnp.float32
    )[..., None]
    pass_sub = (offsets[:, :, -1] >= block_len).astype(jnp.float32)
    pass_dev = (doc_offset[:, -1] >= tok_len).astype(jnp.float32)
    zero_state = jnp.zeros((row_count,) + rate_scale.shape, jnp.float32)
    lag_masks = [(offsets >= lag)[..., None] for lag in range(block_len)]

    def intra_backward(grads):
        total = jnp.zeros_like(grads)
        for lag in range(block_len):
            masked = jnp.where(lag_masks[lag], grads, 0.0)
            padded = jnp.pad(masked, ((0, 0), (0, 0), (0, block_len), (0, 0)))
            total = total + filter_taps[lag] * padded[:, :, lag : lag + block_len, :]
        return total

    def sweep(initial, terms, reverse_flag):
        carried = initial
        visited = [None] * sub_count
        order = range(sub_count - 1, -1, -1) if reverse_flag else range(sub_count)
        for sub_index in order:
            visited[sub_index] = carried
            passed = pass_sub[:, sub_index][:, None, None]
            carried = terms[sub_index] + decay_block * passed * carried
        return carried, jnp.stack(visited)

    mixed = key_short * value_short
    mixed_blocks = mixed.reshape(row_count, sub_count, block_len, channels)
    intra_padded = jnp.pad(mixed_blocks, ((0, 0), (0, 0), (block_len, 0), (0, 0)))
    total = jnp.zeros_like(mixed_blocks)
    for intra_lag in range(block_len):
        shifted = intra_padded[:, :, block_len - intra_lag : 2 * block_len - intra_lag, :]
        total = total + filter_taps[intra_lag] * jnp.where(lag_masks[intra_lag], shifted, 0.0)
    sigma = jnp.swapaxes(
        jnp.sum(pow_end[None, None] * (mixed_blocks * last_doc)[:, :, :, None, :], axis=2), 0, 1
    )
    block_sum, _ = sweep(zero_state, sigma, False)
    states = device_scan(doc_offset[:, -1], block_sum, tok_len * lam_log, 1, tok_len)
    _, enters = sweep(states, sigma, False)
    cross = valid_in * jnp.sum(
        (mode_coef[None] * pow_one)[None, None] * jnp.swapaxes(enters, 0, 1)[:, :, None], axis=3
    )
    long_out = (total + cross).reshape(row_count, tok_len, channels)
    z_full = long_out + skip_gain * mixed
    mixed_out = (query_short * z_full).astype(jnp.bfloat16)
    grad_in = out_grad.astype(jnp.float32)
    z_grad = grad_in * query_short
    query_short_grad = grad_in * z_full
    grad_blocks = z_grad.reshape(row_count, sub_count, block_len, channels)
    inner_back = intra_backward(grad_blocks)
    gamma = jnp.swapaxes(
        jnp.sum(pow_zero[None, None] * (grad_blocks * valid_in)[:, :, :, None, :], axis=2), 0, 1
    )
    block_adj, _ = sweep(zero_state, gamma, True)
    adj_in = device_scan(doc_offset[:, 0], block_adj, tok_len * lam_log, -1, tok_len)
    _, exits = sweep(adj_in, gamma, True)
    cross_back = last_doc * jnp.sum(
        (mode_coef[None] * pow_back)[None, None] * jnp.swapaxes(exits, 0, 1)[:, :, None], axis=3
    )
    mixed_grad = (inner_back + cross_back).reshape(
        row_count, tok_len, channels
    ) + skip_gain * z_grad
    key_short_grad = mixed_grad * value_short
    value_short_grad = mixed_grad * key_short
    padded_mixed = jnp.pad(mixed_blocks, ((0, 0), (0, 0), (block_len, 0), (0, 0)))
    lag_sums = jnp.stack(
        [
            jnp.sum(
                grad_blocks
                * jnp.where(
                    lag_masks[lag],
                    padded_mixed[:, :, block_len - lag : 2 * block_len - lag, :],
                    0.0,
                ),
                axis=(0, 1, 2),
            )
            for lag in range(block_len)
        ],
        axis=0,
    )
    residue_term = norm_factor * (
        jnp.sum(lag_sums[:, None, :] * pow_zero, axis=0)
        + jnp.sum(decay_step[None, None] * gamma * enters, axis=(0, 1))
    )
    skip_term = jnp.sum(z_grad * mixed, axis=(0, 1))
    short_grads = jnp.stack([query_short_grad, key_short_grad, value_short_grad], axis=0)
    spread = jnp.zeros((3, row_count, tok_len + rim_len, channels), jnp.float32)
    tap_terms = []
    for tap_index in range(tap_count):
        masked = jnp.where(tap_masks[tap_index], short_grads, 0.0)
        padded = jnp.pad(masked, ((0, 0), (0, 0), (rim_len, rim_len), (0, 0)))
        spread = (
            spread
            + short_taps[:, tap_index][:, None, None, :]
            * padded[:, :, tap_index : tap_index + tok_len + rim_len, :]
        )
    heads = spread[:, :, :rim_len, :]
    owns = spread[:, :, rim_len:, :]
    incoming = from_behind((heads[0], heads[1], heads[2]), "ctx", -1)
    input_grads = [
        (
            owns[branch_index]
            + jnp.pad(incoming[branch_index], ((0, 0), (tok_len - rim_len, 0), (0, 0)))
        ).astype(jnp.bfloat16)
        for branch_index in range(3)
    ]
    query_taps = jnp.stack(
        [jnp.sum(window(tap_index)[0] * query_short_grad, axis=(0, 1)) for tap_index in range(tap_count)]
    )
    early = jnp.concatenate([query_taps.reshape(-1), skip_term, residue_term.reshape(-1)])
    early = spread_sum(early, "ctx", ("dp",))
    late_taps = jnp.stack(
        [
            jnp.sum(window(tap_index)[1:] * short_grads[1:], axis=(1, 2))
            for tap_index in range(tap_count)
        ],
        axis=1,
    )
    late = spread_sum(late_taps.reshape(-1), "ctx", ("dp",))
    taps_sum = jnp.concatenate(
        [early[: query_taps.size].reshape((1,) + query_taps.shape), late.reshape(late_taps.shape)]
    )
    skip_sum = early[query_taps.size : query_taps.size + skip_term.size]
    residue_sum = early[query_taps.size + skip_term.size :].reshape(residue_term.shape)
    scale = 1.0 / math.sqrt(total_tokens)
    return (
        mixed_out,
        input_grads[0],
        input_grads[1],
        input_grads[2],
        taps_sum * scale,
        skip_sum * scale,
        residue_sum * scale,
    )


def solution(mesh):
    in_specs = (
        P("dp", "ctx", None),
        P("dp", "ctx", None),
        P("dp", "ctx", None),
        P("dp", "ctx"),
        P(),
        P(),
        P(),
        P(),
        P("dp", "ctx", None),
    )
    out_specs = (
        P("dp", "ctx", None),
        P("dp", "ctx", None),
        P("dp", "ctx", None),
        P("dp", "ctx", None),
        P(),
        P(),
        P(),
    )
    return jax.shard_map(shards, mesh=mesh, in_specs=in_specs, out_specs=out_specs, check_vma=False)
```

```python
import math

import jax
import jax.numpy as jnp
from jax import lax
from jax.sharding import PartitionSpec as P


def from_behind(block, axis, distance):
    devices = range(lax.axis_size(axis))
    route = [(i - distance, i) for i in devices if i - distance in devices]
    return lax.ppermute(block, axis, route)


def device_scan(firsts, lasts, values, step_log, direction, tok_len):
    count = lax.axis_size("ctx")

    def moved(block, distance):
        route = [(i, i + distance * direction) for i in range(count) if 0 <= i + distance * direction < count]
        return lax.ppermute(block, "ctx", route)

    def gate(condition):
        return condition.astype(jnp.float32)[:, None, None]

    sums = moved(values, 1)
    if count <= 2:
        return sums
    if direction > 0:
        sums = sums + gate(firsts > tok_len) * jnp.exp(step_log) * moved(values, 2)
    else:
        sums = sums + jnp.exp(step_log) * moved(gate(firsts > tok_len) * values, 2)
    distance = 2
    while distance < count:
        if direction > 0:
            sums = sums + gate(firsts > distance * tok_len) * jnp.exp(distance * step_log) * moved(sums, distance)
        else:
            sums = sums + jnp.exp(distance * step_log) * moved(gate(lasts >= distance * tok_len) * sums, distance)
        distance *= 2
    return sums


def butterfly_sum(value, axes):
    for axis in axes:
        count = lax.axis_size(axis)
        if count & (count - 1):
            value = lax.psum(value, axis)
            continue
        step = 1
        while step < count:
            value = value + lax.ppermute(value, axis, [(i, i ^ step) for i in range(count)])
            step *= 2
    return value


def spread_sum(value, scatter_axis, other_axes):
    count = lax.axis_size(scatter_axis)
    if count & (count - 1) or value.shape[0] % count:
        return butterfly_sum(value, (scatter_axis,) + tuple(other_axes))
    index = lax.axis_index(scatter_axis)
    lanes = 128 if (value.shape[0] // count) % 128 == 0 else 1
    blocks = value.reshape(count, -1, lanes)
    steps = [1 << bit for bit in range(count.bit_length() - 1)]
    steps = [s for s in steps if s in (1, 4)] + [s for s in steps if s not in (1, 4)]
    for step in steps:
        half = blocks.shape[0] // 2
        low = (index // step) % 2 == 0
        keep = jnp.where(low, blocks[:half], blocks[half:])
        send = jnp.where(low, blocks[half:], blocks[:half])
        blocks = keep + lax.ppermute(send, scatter_axis, [(i, i ^ step) for i in range(count)])
    blocks = butterfly_sum(blocks, other_axes)
    for step in reversed(steps):
        got = lax.ppermute(blocks, scatter_axis, [(i, i ^ step) for i in range(count)])
        low = (index // step) % 2 == 0
        blocks = jnp.where(low, jnp.concatenate([blocks, got]), jnp.concatenate([got, blocks]))
    return blocks.reshape(-1)


def shards(
    query_proj,
    key_proj,
    value_proj,
    doc_offset,
    short_taps,
    rate_scale,
    residue,
    skip_gain,
    out_grad,
):
    row_count, tok_len, channels = query_proj.shape
    ctx_count = lax.axis_size("ctx")
    seq_len = tok_len * ctx_count
    total_tokens = row_count * lax.axis_size("dp") * seq_len
    ctx_index = lax.axis_index("ctx")
    tap_count = short_taps.shape[1]
    rim_len = tap_count - 1
    block_len = math.gcd(tok_len, 16)
    sub_count = tok_len // block_len
    rims = from_behind(
        (
            query_proj[:, tok_len - rim_len :, :],
            key_proj[:, tok_len - rim_len :, :],
            value_proj[:, tok_len - rim_len :, :],
        ),
        "ctx",
        1,
    )
    sources = (query_proj, key_proj, value_proj)
    extended = jnp.stack(
        [
            jnp.concatenate([rims[branch_index], sources[branch_index]], axis=1)
            for branch_index in range(3)
        ],
        axis=0,
    )
    tap_masks = [(doc_offset >= tap_index)[None, :, :, None] for tap_index in range(tap_count)]

    def window(tap_index):
        piece = extended[:, :, rim_len - tap_index : rim_len - tap_index + tok_len, :].astype(
            jnp.float32
        )
        return jnp.where(tap_masks[tap_index], piece, 0.0)

    shorts = jnp.zeros((3, row_count, tok_len, channels), jnp.float32)
    for tap_index in range(tap_count):
        shorts = shorts + short_taps[:, tap_index][:, None, None, :] * window(tap_index)
    query_short = shorts[0]
    key_short = shorts[1]
    value_short = shorts[2]
    lam_log = -rate_scale / seq_len
    decay_step = jnp.exp(lam_log)
    norm_factor = jnp.sqrt(-jnp.expm1(2.0 * lam_log))
    mode_coef = residue * norm_factor
    slot_index = jnp.arange(block_len, dtype=jnp.int32)
    slot_float = slot_index.astype(jnp.float32)
    pow_zero = jnp.exp(slot_float[:, None, None] * lam_log[None, :, :])
    pow_one = pow_zero * decay_step[None]
    pow_end = pow_zero[::-1]
    pow_back = pow_one[::-1]
    filter_taps = jnp.sum(mode_coef[None] * pow_zero, axis=1)
    decay_block = jnp.exp(block_len * lam_log)
    offsets = doc_offset.reshape(row_count, sub_count, block_len)
    valid_in = (offsets > slot_index[None, None, :]).astype(jnp.float32)[..., None]
    last_doc = (slot_index[None, None, :] >= block_len - 1 - offsets[:, :, -1:]).astype(
        jnp.float32
    )[..., None]
    pass_sub = (offsets[:, :, -1] >= block_len).astype(jnp.float32)
    pass_dev = (doc_offset[:, -1] >= tok_len).astype(jnp.float32)
    zero_state = jnp.zeros((row_count,) + rate_scale.shape, jnp.float32)
    lag_masks = [(offsets >= lag)[..., None] for lag in range(block_len)]

    def intra_backward(grads):
        total = jnp.zeros_like(grads)
        for lag in range(block_len):
            masked = jnp.where(lag_masks[lag], grads, 0.0)
            padded = jnp.pad(masked, ((0, 0), (0, 0), (0, block_len), (0, 0)))
            total = total + filter_taps[lag] * padded[:, :, lag : lag + block_len, :]
        return total

    def sweep(initial, terms, reverse_flag):
        carried = initial
        visited = [None] * sub_count
        order = range(sub_count - 1, -1, -1) if reverse_flag else range(sub_count)
        for sub_index in order:
            visited[sub_index] = carried
            passed = pass_sub[:, sub_index][:, None, None]
            carried = terms[sub_index] + decay_block * passed * carried
        return carried, jnp.stack(visited)

    mixed = key_short * value_short
    mixed_blocks = mixed.reshape(row_count, sub_count, block_len, channels)
    intra_padded = jnp.pad(mixed_blocks, ((0, 0), (0, 0), (block_len, 0), (0, 0)))
    total = jnp.zeros_like(mixed_blocks)
    for intra_lag in range(block_len):
        shifted = intra_padded[:, :, block_len - intra_lag : 2 * block_len - intra_lag, :]
        total = total + filter_taps[intra_lag] * jnp.where(lag_masks[intra_lag], shifted, 0.0)
    sigma = jnp.swapaxes(
        jnp.sum(pow_end[None, None] * (mixed_blocks * last_doc)[:, :, :, None, :], axis=2), 0, 1
    )
    block_sum, _ = sweep(zero_state, sigma, False)
    states = device_scan(doc_offset[:, 0], doc_offset[:, -1], block_sum, tok_len * lam_log, 1, tok_len)
    _, enters = sweep(states, sigma, False)
    cross = valid_in * jnp.sum(
        (mode_coef[None] * pow_one)[None, None] * jnp.swapaxes(enters, 0, 1)[:, :, None], axis=3
    )
    long_out = (total + cross).reshape(row_count, tok_len, channels)
    z_full = long_out + skip_gain * mixed
    mixed_out = (query_short * z_full).astype(jnp.bfloat16)
    grad_in = out_grad.astype(jnp.float32)
    z_grad = grad_in * query_short
    query_short_grad = grad_in * z_full
    grad_blocks = z_grad.reshape(row_count, sub_count, block_len, channels)
    inner_back = intra_backward(grad_blocks)
    gamma = jnp.swapaxes(
        jnp.sum(pow_zero[None, None] * (grad_blocks * valid_in)[:, :, :, None, :], axis=2), 0, 1
    )
    block_adj, _ = sweep(zero_state, gamma, True)
    adj_in = device_scan(doc_offset[:, 0], doc_offset[:, -1], block_adj, tok_len * lam_log, -1, tok_len)
    _, exits = sweep(adj_in, gamma, True)
    cross_back = last_doc * jnp.sum(
        (mode_coef[None] * pow_back)[None, None] * jnp.swapaxes(exits, 0, 1)[:, :, None], axis=3
    )
    mixed_grad = (inner_back + cross_back).reshape(
        row_count, tok_len, channels
    ) + skip_gain * z_grad
    key_short_grad = mixed_grad * value_short
    value_short_grad = mixed_grad * key_short
    padded_mixed = jnp.pad(mixed_blocks, ((0, 0), (0, 0), (block_len, 0), (0, 0)))
    lag_sums = jnp.stack(
        [
            jnp.sum(
                grad_blocks
                * jnp.where(
                    lag_masks[lag],
                    padded_mixed[:, :, block_len - lag : 2 * block_len - lag, :],
                    0.0,
                ),
                axis=(0, 1, 2),
            )
            for lag in range(block_len)
        ],
        axis=0,
    )
    residue_term = norm_factor * (
        jnp.sum(lag_sums[:, None, :] * pow_zero, axis=0)
        + jnp.sum(decay_step[None, None] * gamma * enters, axis=(0, 1))
    )
    skip_term = jnp.sum(z_grad * mixed, axis=(0, 1))
    short_grads = jnp.stack([query_short_grad, key_short_grad, value_short_grad], axis=0)
    spread = jnp.zeros((3, row_count, tok_len + rim_len, channels), jnp.float32)
    tap_terms = []
    for tap_index in range(tap_count):
        masked = jnp.where(tap_masks[tap_index], short_grads, 0.0)
        padded = jnp.pad(masked, ((0, 0), (0, 0), (rim_len, rim_len), (0, 0)))
        spread = (
            spread
            + short_taps[:, tap_index][:, None, None, :]
            * padded[:, :, tap_index : tap_index + tok_len + rim_len, :]
        )
        tap_terms.append(jnp.sum(window(tap_index) * short_grads, axis=(1, 2)))
    heads = spread[:, :, :rim_len, :]
    owns = spread[:, :, rim_len:, :]
    incoming = from_behind((heads[0], heads[1], heads[2]), "ctx", -1)
    input_grads = [
        (
            owns[branch_index]
            + jnp.pad(incoming[branch_index], ((0, 0), (tok_len - rim_len, 0), (0, 0)))
        ).astype(jnp.bfloat16)
        for branch_index in range(3)
    ]
    tap_stack = jnp.stack(tap_terms, axis=1)
    flat = jnp.concatenate([tap_stack.reshape(-1), skip_term, residue_term.reshape(-1)])
    flat = spread_sum(flat, "ctx", ("dp",))
    taps_sum = flat[: tap_stack.size].reshape(tap_stack.shape)
    skip_sum = flat[tap_stack.size : tap_stack.size + skip_term.size]
    residue_sum = flat[tap_stack.size + skip_term.size :].reshape(residue_term.shape)
    scale = 1.0 / math.sqrt(total_tokens)
    return (
        mixed_out,
        input_grads[0],
        input_grads[1],
        input_grads[2],
        taps_sum * scale,
        skip_sum * scale,
        residue_sum * scale,
    )


def solution(mesh):
    in_specs = (
        P("dp", "ctx", None),
        P("dp", "ctx", None),
        P("dp", "ctx", None),
        P("dp", "ctx"),
        P(),
        P(),
        P(),
        P(),
        P("dp", "ctx", None),
    )
    out_specs = (
        P("dp", "ctx", None),
        P("dp", "ctx", None),
        P("dp", "ctx", None),
        P("dp", "ctx", None),
        P(),
        P(),
        P(),
    )
    return jax.shard_map(shards, mesh=mesh, in_specs=in_specs, out_specs=out_specs, check_vma=False)
```

```python
import math

import jax
import jax.numpy as jnp
from jax import lax
from jax.sharding import PartitionSpec as P


def from_behind(block, axis, distance):
    devices = range(lax.axis_size(axis))
    route = [(i - distance, i) for i in devices if i - distance in devices]
    return lax.ppermute(block, axis, route)


def device_scan(firsts, lasts, values, step_log, direction, tok_len):
    count = lax.axis_size("ctx")

    def moved(block, distance):
        route = [(i, i + distance * direction) for i in range(count) if 0 <= i + distance * direction < count]
        return lax.ppermute(block, "ctx", route)

    def gate(condition):
        return condition.astype(jnp.float32)[:, None, None]

    sums = moved(values, 1)
    if count <= 2:
        return sums
    if direction > 0:
        sums = sums + gate(firsts > tok_len) * jnp.exp(step_log) * moved(values, 2)
    else:
        sums = sums + jnp.exp(step_log) * moved(gate(firsts > tok_len) * values, 2)
    distance = 2
    while distance < count:
        if direction > 0:
            sums = sums + gate(firsts > distance * tok_len) * jnp.exp(distance * step_log) * moved(sums, distance)
        else:
            sums = sums + jnp.exp(distance * step_log) * moved(gate(lasts >= distance * tok_len) * sums, distance)
        distance *= 2
    return sums


def butterfly_sum(value, axes):
    for axis in axes:
        count = lax.axis_size(axis)
        if count & (count - 1):
            value = lax.psum(value, axis)
            continue
        step = 1
        while step < count:
            value = value + lax.ppermute(value, axis, [(i, i ^ step) for i in range(count)])
            step *= 2
    return value


def _digit(index, steps):
    return sum(((index // step) % 2) * (1 << pos) for pos, step in enumerate(steps))


def _mask(offset, steps):
    return sum(step for pos, step in enumerate(steps) if (offset >> pos) & 1)


def _exchange(block, axis, mask):
    return lax.ppermute(block, axis, [(i, i ^ mask) for i in range(lax.axis_size(axis))])


def scatter_stage(blocks, axis, steps, index):
    radix = 1 << len(steps)
    part = blocks.shape[0] // radix
    digit = _digit(index, steps)
    total = lax.dynamic_slice_in_dim(blocks, digit * part, part, axis=0)
    for offset in range(1, radix):
        piece = lax.dynamic_slice_in_dim(blocks, (digit ^ offset) * part, part, axis=0)
        total = total + _exchange(piece, axis, _mask(offset, steps))
    return total


def gather_stage(blocks, axis, steps, index):
    radix = 1 << len(steps)
    digit = _digit(index, steps)
    got = jnp.stack([blocks] + [_exchange(blocks, axis, _mask(o, steps)) for o in range(1, radix)])
    return jnp.concatenate([lax.dynamic_index_in_dim(got, slot ^ digit, keepdims=False) for slot in range(radix)])


def full_sum(value, axis):
    count = lax.axis_size(axis)
    index = lax.axis_index(axis)
    got = jnp.stack([value] + [_exchange(value, axis, o) for o in range(1, count)])
    total = lax.dynamic_index_in_dim(got, index, keepdims=False)
    for member in range(1, count):
        total = total + lax.dynamic_index_in_dim(got, member ^ index, keepdims=False)
    return total


def spread_sum(value, scatter_axis, other_axes):
    count = lax.axis_size(scatter_axis)
    if count & (count - 1) or value.shape[0] % count:
        return butterfly_sum(value, (scatter_axis,) + tuple(other_axes))
    index = lax.axis_index(scatter_axis)
    lanes = 128 if (value.shape[0] // count) % 128 == 0 else 1
    blocks = value.reshape(count, -1, lanes)
    stages = [tuple(s for s in group if s < count) for group in ((1, 2), (4,), (8, 16))]
    stages = [group for group in stages if group]
    stages += [(1 << bit,) for bit in range(5, count.bit_length() - 1)]
    for steps in stages:
        blocks = scatter_stage(blocks, scatter_axis, steps, index)
    for axis in other_axes:
        size = lax.axis_size(axis)
        blocks = full_sum(blocks, axis) if size & (size - 1) == 0 else lax.psum(blocks, axis)
    for steps in reversed(stages):
        blocks = gather_stage(blocks, scatter_axis, steps, index)
    return blocks.reshape(-1)


def shards(
    query_proj,
    key_proj,
    value_proj,
    doc_offset,
    short_taps,
    rate_scale,
    residue,
    skip_gain,
    out_grad,
):
    row_count, tok_len, channels = query_proj.shape
    ctx_count = lax.axis_size("ctx")
    seq_len = tok_len * ctx_count
    total_tokens = row_count * lax.axis_size("dp") * seq_len
    ctx_index = lax.axis_index("ctx")
    tap_count = short_taps.shape[1]
    rim_len = tap_count - 1
    block_len = math.gcd(tok_len, 16)
    sub_count = tok_len // block_len
    rims = from_behind(
        (
            query_proj[:, tok_len - rim_len :, :],
            key_proj[:, tok_len - rim_len :, :],
            value_proj[:, tok_len - rim_len :, :],
        ),
        "ctx",
        1,
    )
    sources = (query_proj, key_proj, value_proj)
    extended = jnp.stack(
        [
            jnp.concatenate([rims[branch_index], sources[branch_index]], axis=1)
            for branch_index in range(3)
        ],
        axis=0,
    )
    tap_masks = [(doc_offset >= tap_index)[None, :, :, None] for tap_index in range(tap_count)]

    def window(tap_index):
        piece = extended[:, :, rim_len - tap_index : rim_len - tap_index + tok_len, :].astype(
            jnp.float32
        )
        return jnp.where(tap_masks[tap_index], piece, 0.0)

    shorts = jnp.zeros((3, row_count, tok_len, channels), jnp.float32)
    for tap_index in range(tap_count):
        shorts = shorts + short_taps[:, tap_index][:, None, None, :] * window(tap_index)
    query_short = shorts[0]
    key_short = shorts[1]
    value_short = shorts[2]
    lam_log = -rate_scale / seq_len
    decay_step = jnp.exp(lam_log)
    norm_factor = jnp.sqrt(-jnp.expm1(2.0 * lam_log))
    mode_coef = residue * norm_factor
    slot_index = jnp.arange(block_len, dtype=jnp.int32)
    slot_float = slot_index.astype(jnp.float32)
    pow_zero = jnp.exp(slot_float[:, None, None] * lam_log[None, :, :])
    pow_one = pow_zero * decay_step[None]
    pow_end = pow_zero[::-1]
    pow_back = pow_one[::-1]
    filter_taps = jnp.sum(mode_coef[None] * pow_zero, axis=1)
    decay_block = jnp.exp(block_len * lam_log)
    offsets = doc_offset.reshape(row_count, sub_count, block_len)
    valid_in = (offsets > slot_index[None, None, :]).astype(jnp.float32)[..., None]
    last_doc = (slot_index[None, None, :] >= block_len - 1 - offsets[:, :, -1:]).astype(
        jnp.float32
    )[..., None]
    pass_sub = (offsets[:, :, -1] >= block_len).astype(jnp.float32)
    pass_dev = (doc_offset[:, -1] >= tok_len).astype(jnp.float32)
    zero_state = jnp.zeros((row_count,) + rate_scale.shape, jnp.float32)
    lag_masks = [(offsets >= lag)[..., None] for lag in range(block_len)]

    def intra_backward(grads):
        total = jnp.zeros_like(grads)
        for lag in range(block_len):
            masked = jnp.where(lag_masks[lag], grads, 0.0)
            padded = jnp.pad(masked, ((0, 0), (0, 0), (0, block_len), (0, 0)))
            total = total + filter_taps[lag] * padded[:, :, lag : lag + block_len, :]
        return total

    def sweep(initial, terms, reverse_flag):
        carried = initial
        visited = [None] * sub_count
        order = range(sub_count - 1, -1, -1) if reverse_flag else range(sub_count)
        for sub_index in order:
            visited[sub_index] = carried
            passed = pass_sub[:, sub_index][:, None, None]
            carried = terms[sub_index] + decay_block * passed * carried
        return carried, jnp.stack(visited)

    mixed = key_short * value_short
    mixed_blocks = mixed.reshape(row_count, sub_count, block_len, channels)
    intra_padded = jnp.pad(mixed_blocks, ((0, 0), (0, 0), (block_len, 0), (0, 0)))
    total = jnp.zeros_like(mixed_blocks)
    for intra_lag in range(block_len):
        shifted = intra_padded[:, :, block_len - intra_lag : 2 * block_len - intra_lag, :]
        total = total + filter_taps[intra_lag] * jnp.where(lag_masks[intra_lag], shifted, 0.0)
    sigma = jnp.swapaxes(
        jnp.sum(pow_end[None, None] * (mixed_blocks * last_doc)[:, :, :, None, :], axis=2), 0, 1
    )
    block_sum, _ = sweep(zero_state, sigma, False)
    states = device_scan(doc_offset[:, 0], doc_offset[:, -1], block_sum, tok_len * lam_log, 1, tok_len)
    _, enters = sweep(states, sigma, False)
    cross = valid_in * jnp.sum(
        (mode_coef[None] * pow_one)[None, None] * jnp.swapaxes(enters, 0, 1)[:, :, None], axis=3
    )
    long_out = (total + cross).reshape(row_count, tok_len, channels)
    z_full = long_out + skip_gain * mixed
    mixed_out = (query_short * z_full).astype(jnp.bfloat16)
    grad_in = out_grad.astype(jnp.float32)
    z_grad = grad_in * query_short
    query_short_grad = grad_in * z_full
    grad_blocks = z_grad.reshape(row_count, sub_count, block_len, channels)
    inner_back = intra_backward(grad_blocks)
    gamma = jnp.swapaxes(
        jnp.sum(pow_zero[None, None] * (grad_blocks * valid_in)[:, :, :, None, :], axis=2), 0, 1
    )
    block_adj, _ = sweep(zero_state, gamma, True)
    adj_in = device_scan(doc_offset[:, 0], doc_offset[:, -1], block_adj, tok_len * lam_log, -1, tok_len)
    _, exits = sweep(adj_in, gamma, True)
    cross_back = last_doc * jnp.sum(
        (mode_coef[None] * pow_back)[None, None] * jnp.swapaxes(exits, 0, 1)[:, :, None], axis=3
    )
    mixed_grad = (inner_back + cross_back).reshape(
        row_count, tok_len, channels
    ) + skip_gain * z_grad
    key_short_grad = mixed_grad * value_short
    value_short_grad = mixed_grad * key_short
    padded_mixed = jnp.pad(mixed_blocks, ((0, 0), (0, 0), (block_len, 0), (0, 0)))
    lag_sums = jnp.stack(
        [
            jnp.sum(
                grad_blocks
                * jnp.where(
                    lag_masks[lag],
                    padded_mixed[:, :, block_len - lag : 2 * block_len - lag, :],
                    0.0,
                ),
                axis=(0, 1, 2),
            )
            for lag in range(block_len)
        ],
        axis=0,
    )
    residue_term = norm_factor * (
        jnp.sum(lag_sums[:, None, :] * pow_zero, axis=0)
        + jnp.sum(decay_step[None, None] * gamma * enters, axis=(0, 1))
    )
    skip_term = jnp.sum(z_grad * mixed, axis=(0, 1))
    short_grads = jnp.stack([query_short_grad, key_short_grad, value_short_grad], axis=0)
    spread = jnp.zeros((3, row_count, tok_len + rim_len, channels), jnp.float32)
    tap_terms = []
    for tap_index in range(tap_count):
        masked = jnp.where(tap_masks[tap_index], short_grads, 0.0)
        padded = jnp.pad(masked, ((0, 0), (0, 0), (rim_len, rim_len), (0, 0)))
        spread = (
            spread
            + short_taps[:, tap_index][:, None, None, :]
            * padded[:, :, tap_index : tap_index + tok_len + rim_len, :]
        )
        tap_terms.append(jnp.sum(window(tap_index) * short_grads, axis=(1, 2)))
    heads = spread[:, :, :rim_len, :]
    owns = spread[:, :, rim_len:, :]
    incoming = from_behind((heads[0], heads[1], heads[2]), "ctx", -1)
    input_grads = [
        (
            owns[branch_index]
            + jnp.pad(incoming[branch_index], ((0, 0), (tok_len - rim_len, 0), (0, 0)))
        ).astype(jnp.bfloat16)
        for branch_index in range(3)
    ]
    tap_stack = jnp.stack(tap_terms, axis=1)
    flat = jnp.concatenate([tap_stack.reshape(-1), skip_term, residue_term.reshape(-1)])
    flat = spread_sum(flat, "ctx", ("dp",))
    taps_sum = flat[: tap_stack.size].reshape(tap_stack.shape)
    skip_sum = flat[tap_stack.size : tap_stack.size + skip_term.size]
    residue_sum = flat[tap_stack.size + skip_term.size :].reshape(residue_term.shape)
    scale = 1.0 / math.sqrt(total_tokens)
    return (
        mixed_out,
        input_grads[0],
        input_grads[1],
        input_grads[2],
        taps_sum * scale,
        skip_sum * scale,
        residue_sum * scale,
    )


def solution(mesh):
    in_specs = (
        P("dp", "ctx", None),
        P("dp", "ctx", None),
        P("dp", "ctx", None),
        P("dp", "ctx"),
        P(),
        P(),
        P(),
        P(),
        P("dp", "ctx", None),
    )
    out_specs = (
        P("dp", "ctx", None),
        P("dp", "ctx", None),
        P("dp", "ctx", None),
        P("dp", "ctx", None),
        P(),
        P(),
        P(),
    )
    return jax.shard_map(shards, mesh=mesh, in_specs=in_specs, out_specs=out_specs, check_vma=False)
```

```python
import math

import jax
import jax.numpy as jnp
from jax import lax
from jax.sharding import PartitionSpec as P


def from_behind(block, axis, distance):
    devices = range(lax.axis_size(axis))
    route = [(i - distance, i) for i in devices if i - distance in devices]
    return lax.ppermute(block, axis, route)


def device_scan(firsts, lasts, values, step_log, direction, tok_len):
    count = lax.axis_size("ctx")

    def moved(block, distance):
        route = [(i, i + distance * direction) for i in range(count) if 0 <= i + distance * direction < count]
        return lax.ppermute(block, "ctx", route)

    def gate(condition):
        return condition.astype(jnp.float32)[:, None, None]

    sums = moved(values, 1)
    for lag in range(2, min(4, count - 1) + 1):
        if direction > 0:
            sums = sums + gate(firsts > (lag - 1) * tok_len) * jnp.exp((lag - 1) * step_log) * moved(values, lag)
        else:
            sums = sums + jnp.exp((lag - 1) * step_log) * moved(gate(firsts > (lag - 1) * tok_len) * values, lag)
    span = 4
    while span < count:
        radix = min(4, count // span)
        total = sums
        for part in range(1, radix):
            reach = part * span
            if direction > 0:
                total = total + gate(firsts > reach * tok_len) * jnp.exp(reach * step_log) * moved(sums, reach)
            else:
                total = total + jnp.exp(reach * step_log) * moved(gate(lasts >= reach * tok_len) * sums, reach)
        sums = total
        span *= radix
    return sums


def butterfly_sum(value, axes):
    for axis in axes:
        count = lax.axis_size(axis)
        if count & (count - 1):
            value = lax.psum(value, axis)
            continue
        step = 1
        while step < count:
            value = value + lax.ppermute(value, axis, [(i, i ^ step) for i in range(count)])
            step *= 2
    return value


def _digit(index, steps):
    return sum(((index // step) % 2) * (1 << pos) for pos, step in enumerate(steps))


def _mask(offset, steps):
    return sum(step for pos, step in enumerate(steps) if (offset >> pos) & 1)


def _exchange(block, axis, mask):
    return lax.ppermute(block, axis, [(i, i ^ mask) for i in range(lax.axis_size(axis))])


def scatter_stage(blocks, axis, steps, index):
    radix = 1 << len(steps)
    part = blocks.shape[0] // radix
    digit = _digit(index, steps)
    total = lax.dynamic_slice_in_dim(blocks, digit * part, part, axis=0)
    for offset in range(1, radix):
        piece = lax.dynamic_slice_in_dim(blocks, (digit ^ offset) * part, part, axis=0)
        total = total + _exchange(piece, axis, _mask(offset, steps))
    return total


def gather_stage(blocks, axis, steps, index):
    radix = 1 << len(steps)
    digit = _digit(index, steps)
    got = jnp.stack([blocks] + [_exchange(blocks, axis, _mask(o, steps)) for o in range(1, radix)])
    return jnp.concatenate([lax.dynamic_index_in_dim(got, slot ^ digit, keepdims=False) for slot in range(radix)])


def full_sum(value, axis):
    count = lax.axis_size(axis)
    index = lax.axis_index(axis)
    got = jnp.stack([value] + [_exchange(value, axis, o) for o in range(1, count)])
    total = lax.dynamic_index_in_dim(got, index, keepdims=False)
    for member in range(1, count):
        total = total + lax.dynamic_index_in_dim(got, member ^ index, keepdims=False)
    return total


def spread_sum(value, scatter_axis, other_axes):
    count = lax.axis_size(scatter_axis)
    if count & (count - 1) or value.shape[0] % count:
        return butterfly_sum(value, (scatter_axis,) + tuple(other_axes))
    index = lax.axis_index(scatter_axis)
    lanes = 128 if (value.shape[0] // count) % 128 == 0 else 1
    blocks = value.reshape(count, -1, lanes)
    stages = [tuple(s for s in group if s < count) for group in ((1, 2), (4,), (8, 16))]
    stages = [group for group in stages if group]
    stages += [(1 << bit,) for bit in range(5, count.bit_length() - 1)]
    for steps in stages:
        blocks = scatter_stage(blocks, scatter_axis, steps, index)
    for axis in other_axes:
        size = lax.axis_size(axis)
        blocks = full_sum(blocks, axis) if size & (size - 1) == 0 else lax.psum(blocks, axis)
    for steps in reversed(stages):
        blocks = gather_stage(blocks, scatter_axis, steps, index)
    return blocks.reshape(-1)


def shards(
    query_proj,
    key_proj,
    value_proj,
    doc_offset,
    short_taps,
    rate_scale,
    residue,
    skip_gain,
    out_grad,
):
    row_count, tok_len, channels = query_proj.shape
    ctx_count = lax.axis_size("ctx")
    seq_len = tok_len * ctx_count
    total_tokens = row_count * lax.axis_size("dp") * seq_len
    ctx_index = lax.axis_index("ctx")
    tap_count = short_taps.shape[1]
    rim_len = tap_count - 1
    block_len = math.gcd(tok_len, 16)
    sub_count = tok_len // block_len
    rims = from_behind(
        (
            query_proj[:, tok_len - rim_len :, :],
            key_proj[:, tok_len - rim_len :, :],
            value_proj[:, tok_len - rim_len :, :],
        ),
        "ctx",
        1,
    )
    sources = (query_proj, key_proj, value_proj)
    extended = jnp.stack(
        [
            jnp.concatenate([rims[branch_index], sources[branch_index]], axis=1)
            for branch_index in range(3)
        ],
        axis=0,
    )
    tap_masks = [(doc_offset >= tap_index)[None, :, :, None] for tap_index in range(tap_count)]

    def window(tap_index):
        piece = extended[:, :, rim_len - tap_index : rim_len - tap_index + tok_len, :].astype(
            jnp.float32
        )
        return jnp.where(tap_masks[tap_index], piece, 0.0)

    shorts = jnp.zeros((3, row_count, tok_len, channels), jnp.float32)
    for tap_index in range(tap_count):
        shorts = shorts + short_taps[:, tap_index][:, None, None, :] * window(tap_index)
    query_short = shorts[0]
    key_short = shorts[1]
    value_short = shorts[2]
    lam_log = -rate_scale / seq_len
    decay_step = jnp.exp(lam_log)
    norm_factor = jnp.sqrt(-jnp.expm1(2.0 * lam_log))
    mode_coef = residue * norm_factor
    slot_index = jnp.arange(block_len, dtype=jnp.int32)
    slot_float = slot_index.astype(jnp.float32)
    pow_zero = jnp.exp(slot_float[:, None, None] * lam_log[None, :, :])
    pow_one = pow_zero * decay_step[None]
    pow_end = pow_zero[::-1]
    pow_back = pow_one[::-1]
    filter_taps = jnp.sum(mode_coef[None] * pow_zero, axis=1)
    decay_block = jnp.exp(block_len * lam_log)
    offsets = doc_offset.reshape(row_count, sub_count, block_len)
    valid_in = (offsets > slot_index[None, None, :]).astype(jnp.float32)[..., None]
    last_doc = (slot_index[None, None, :] >= block_len - 1 - offsets[:, :, -1:]).astype(
        jnp.float32
    )[..., None]
    pass_sub = (offsets[:, :, -1] >= block_len).astype(jnp.float32)
    pass_dev = (doc_offset[:, -1] >= tok_len).astype(jnp.float32)
    zero_state = jnp.zeros((row_count,) + rate_scale.shape, jnp.float32)
    lag_masks = [(offsets >= lag)[..., None] for lag in range(block_len)]

    def intra_backward(grads):
        total = jnp.zeros_like(grads)
        for lag in range(block_len):
            masked = jnp.where(lag_masks[lag], grads, 0.0)
            padded = jnp.pad(masked, ((0, 0), (0, 0), (0, block_len), (0, 0)))
            total = total + filter_taps[lag] * padded[:, :, lag : lag + block_len, :]
        return total

    def sweep(initial, terms, reverse_flag):
        carried = initial
        visited = [None] * sub_count
        order = range(sub_count - 1, -1, -1) if reverse_flag else range(sub_count)
        for sub_index in order:
            visited[sub_index] = carried
            passed = pass_sub[:, sub_index][:, None, None]
            carried = terms[sub_index] + decay_block * passed * carried
        return carried, jnp.stack(visited)

    mixed = key_short * value_short
    mixed_blocks = mixed.reshape(row_count, sub_count, block_len, channels)
    intra_padded = jnp.pad(mixed_blocks, ((0, 0), (0, 0), (block_len, 0), (0, 0)))
    total = jnp.zeros_like(mixed_blocks)
    for intra_lag in range(block_len):
        shifted = intra_padded[:, :, block_len - intra_lag : 2 * block_len - intra_lag, :]
        total = total + filter_taps[intra_lag] * jnp.where(lag_masks[intra_lag], shifted, 0.0)
    sigma = jnp.swapaxes(
        jnp.sum(pow_end[None, None] * (mixed_blocks * last_doc)[:, :, :, None, :], axis=2), 0, 1
    )
    block_sum, _ = sweep(zero_state, sigma, False)
    states = device_scan(doc_offset[:, 0], doc_offset[:, -1], block_sum, tok_len * lam_log, 1, tok_len)
    _, enters = sweep(states, sigma, False)
    cross = valid_in * jnp.sum(
        (mode_coef[None] * pow_one)[None, None] * jnp.swapaxes(enters, 0, 1)[:, :, None], axis=3
    )
    long_out = (total + cross).reshape(row_count, tok_len, channels)
    z_full = long_out + skip_gain * mixed
    mixed_out = (query_short * z_full).astype(jnp.bfloat16)
    grad_in = out_grad.astype(jnp.float32)
    z_grad = grad_in * query_short
    query_short_grad = grad_in * z_full
    grad_blocks = z_grad.reshape(row_count, sub_count, block_len, channels)
    inner_back = intra_backward(grad_blocks)
    gamma = jnp.swapaxes(
        jnp.sum(pow_zero[None, None] * (grad_blocks * valid_in)[:, :, :, None, :], axis=2), 0, 1
    )
    block_adj, _ = sweep(zero_state, gamma, True)
    adj_in = device_scan(doc_offset[:, 0], doc_offset[:, -1], block_adj, tok_len * lam_log, -1, tok_len)
    _, exits = sweep(adj_in, gamma, True)
    cross_back = last_doc * jnp.sum(
        (mode_coef[None] * pow_back)[None, None] * jnp.swapaxes(exits, 0, 1)[:, :, None], axis=3
    )
    mixed_grad = (inner_back + cross_back).reshape(
        row_count, tok_len, channels
    ) + skip_gain * z_grad
    key_short_grad = mixed_grad * value_short
    value_short_grad = mixed_grad * key_short
    padded_mixed = jnp.pad(mixed_blocks, ((0, 0), (0, 0), (block_len, 0), (0, 0)))
    lag_sums = jnp.stack(
        [
            jnp.sum(
                grad_blocks
                * jnp.where(
                    lag_masks[lag],
                    padded_mixed[:, :, block_len - lag : 2 * block_len - lag, :],
                    0.0,
                ),
                axis=(0, 1, 2),
            )
            for lag in range(block_len)
        ],
        axis=0,
    )
    residue_term = norm_factor * (
        jnp.sum(lag_sums[:, None, :] * pow_zero, axis=0)
        + jnp.sum(decay_step[None, None] * gamma * enters, axis=(0, 1))
    )
    skip_term = jnp.sum(z_grad * mixed, axis=(0, 1))
    short_grads = jnp.stack([query_short_grad, key_short_grad, value_short_grad], axis=0)
    spread = jnp.zeros((3, row_count, tok_len + rim_len, channels), jnp.float32)
    tap_terms = []
    for tap_index in range(tap_count):
        masked = jnp.where(tap_masks[tap_index], short_grads, 0.0)
        padded = jnp.pad(masked, ((0, 0), (0, 0), (rim_len, rim_len), (0, 0)))
        spread = (
            spread
            + short_taps[:, tap_index][:, None, None, :]
            * padded[:, :, tap_index : tap_index + tok_len + rim_len, :]
        )
        tap_terms.append(jnp.sum(window(tap_index) * short_grads, axis=(1, 2)))
    heads = spread[:, :, :rim_len, :]
    owns = spread[:, :, rim_len:, :]
    incoming = from_behind((heads[0], heads[1], heads[2]), "ctx", -1)
    input_grads = [
        (
            owns[branch_index]
            + jnp.pad(incoming[branch_index], ((0, 0), (tok_len - rim_len, 0), (0, 0)))
        ).astype(jnp.bfloat16)
        for branch_index in range(3)
    ]
    tap_stack = jnp.stack(tap_terms, axis=1)
    flat = jnp.concatenate([tap_stack.reshape(-1), skip_term, residue_term.reshape(-1)])
    flat = spread_sum(flat, "ctx", ("dp",))
    taps_sum = flat[: tap_stack.size].reshape(tap_stack.shape)
    skip_sum = flat[tap_stack.size : tap_stack.size + skip_term.size]
    residue_sum = flat[tap_stack.size + skip_term.size :].reshape(residue_term.shape)
    scale = 1.0 / math.sqrt(total_tokens)
    return (
        mixed_out,
        input_grads[0],
        input_grads[1],
        input_grads[2],
        taps_sum * scale,
        skip_sum * scale,
        residue_sum * scale,
    )


def solution(mesh):
    in_specs = (
        P("dp", "ctx", None),
        P("dp", "ctx", None),
        P("dp", "ctx", None),
        P("dp", "ctx"),
        P(),
        P(),
        P(),
        P(),
        P("dp", "ctx", None),
    )
    out_specs = (
        P("dp", "ctx", None),
        P("dp", "ctx", None),
        P("dp", "ctx", None),
        P("dp", "ctx", None),
        P(),
        P(),
        P(),
    )
    return jax.shard_map(shards, mesh=mesh, in_specs=in_specs, out_specs=out_specs, check_vma=False)
```
